256 devices in a mesh: pix: 32 (over z, x), feat: 8 (over y, core).
Axes of the slice: x: 4, y: 4, z: 8, core: 2. Of those that a mesh axis runs over, the one named last changes fastest.
Arguments:
- mass_bin: int32 [262144, 256], P(('pix', 'feat')), may hold values from 0 to 255
- mobility_bin: int32 [262144, 256], P(('pix', 'feat')), may hold values from 0 to 15
- intensity: bfloat16 [262144, 256], P(('pix', 'feat')), may hold values from 10 to 4000, as said below
- basis_init: float32 [262144, 64], P(('pix', 'feat')), may hold values from 0.1 to 1
- profile_init: float32 [64, 4096], P(None, 'feat'), may hold values from 0.1 to 1
Outputs:
- basis: float32 [262144, 64], P(('pix', 'feat'))
- profiles: float32 [64, 4096], P(None, 'feat')
The draws below stay inside these ranges and needn't reach their ends.
Inputs may be any that keep to these rules, and one draw needn't show every extreme that they name: `intensity`: positive peak intensities.
All inputs are finite; a program needn't handle non-finite values.
Results may differ from the reference program's by a relative error of at most 0.00045.
Values may be sent and summed in bfloat16 or wider, within the bound.
No kernel may reach another device: no remote copies, remote signals or barrier semaphores. Data moves between devices by JAX's collectives and lax.ppermute only.
A program may use at most 64 MiB of HBM per device.

```python
import math
import jax
import jax.numpy as jnp
from jax import lax

MZ = 256
MOB = 16
RANK = 64
PEAKS = 256
ITERS = 2
FEATS = 4096
PIXELS = 262144


def draw_intensity(key, part):
    rows = jnp.arange(PIXELS, dtype=jnp.float32)[:, None] / PIXELS
    scale = 0.3 * jnp.exp(rows * jnp.log(10.0))
    values = jnp.exp(jax.random.uniform(key, (PIXELS, PEAKS), jnp.float32, jnp.log(50.0), jnp.log(1000.0)))
    return (values * scale).astype(jnp.bfloat16)


def plant(array, own_key, least, high):
    longest = array.shape.index(max(array.shape))
    spots = []
    for shift in (0, 1):
        where = [jax.random.randint(jax.random.fold_in(own_key, axis), (), 0, length) for axis, length in enumerate(array.shape)]
        where[longest] = (where[longest] + shift) % array.shape[longest]
        spots.append(tuple(where))
    return array.at[spots[0]].set(least).at[spots[1]].set(high)


def shard_levels(stream_key, shape, cuts, least, top_value):
    loudness, own = 1.0, jax.random.fold_in(stream_key, 6)
    for dim, parts in cuts:
        heights = jnp.exp(jax.random.uniform(jax.random.fold_in(own, dim), (parts,), jnp.float32, least / len(cuts), top_value / len(cuts)))
        loudness = loudness * jnp.repeat(heights, shape[dim] // parts).reshape([-1 if axis == dim else 1 for axis in range(len(shape))])
    return loudness


def setup_inputs(seed: int = 0) -> dict:
    splits = jax.random.split(jax.random.key(seed), 6)
    mass_bin = plant(jax.random.randint(splits[0], (PIXELS, PEAKS), 0, MZ), jax.random.fold_in(splits[0], 1), 0, MZ - 1).astype(jnp.int32)
    mobility_bin = plant(jax.random.randint(splits[1], (PIXELS, PEAKS), 0, MOB), jax.random.fold_in(splits[1], 1), 0, MOB - 1).astype(jnp.int32)
    intensity = draw_intensity(jax.random.fold_in(splits[5], 71), 0)
    basis_init = jnp.clip(0.1 + 0.9 * jax.random.uniform(splits[3], (PIXELS, RANK), jnp.float32) ** shard_levels(splits[3], (PIXELS, RANK), ((0, 256),), -0.2, 0.2), 0.1, 1.0)
    profile_init = jnp.clip(0.1 + 0.9 * jax.random.uniform(splits[4], (RANK, FEATS), jnp.float32) ** shard_levels(splits[4], (RANK, FEATS), ((1, 8),), -0.2, 0.2), 0.1, 1.0)
    return dict(mass_bin=mass_bin, mobility_bin=mobility_bin, intensity=intensity, basis_init=basis_init, profile_init=profile_init)


EPS = 1e-6


def bin_block(args):
    mass, mobility, weight = args
    feature = (mobility * MZ + mass).astype(jnp.int32)
    rows = jnp.broadcast_to(jnp.arange(mass.shape[0], dtype=jnp.int32)[:, None], mass.shape)
    dense = jnp.zeros((mass.shape[0], MZ * MOB), jnp.float32)
    dense = dense.at[rows, feature].add(weight.astype(jnp.float32))
    return dense.astype(jnp.bfloat16)


def reference(mass_bin, mobility_bin, intensity, basis_init, profile_init):
    block = math.gcd(PIXELS, 4096)
    count = PIXELS // block
    spectra = lax.map(bin_block, (mass_bin.reshape(count, block, PEAKS), mobility_bin.reshape(count, block, PEAKS), intensity.reshape(count, block, PEAKS)))
    spectra = spectra.reshape(PIXELS, MZ * MOB)
    basis, profiles = basis_init, profile_init
    highest = lax.Precision.HIGHEST
    for step in range(ITERS):
        numer_h = lax.dot_general(basis.astype(jnp.bfloat16), spectra, (((0,), (0,)), ((), ())), preferred_element_type=jnp.float32)
        gram_w = lax.dot_general(basis, basis, (((0,), (0,)), ((), ())), precision=highest, preferred_element_type=jnp.float32)
        profiles = profiles * numer_h / (jnp.dot(gram_w, profiles, precision=highest, preferred_element_type=jnp.float32) + EPS)
        numer_w = lax.dot_general(spectra, profiles.astype(jnp.bfloat16), (((1,), (1,)), ((), ())), preferred_element_type=jnp.float32)
        gram_h = lax.dot_general(profiles, profiles, (((1,), (1,)), ((), ())), precision=highest, preferred_element_type=jnp.float32)
        basis = basis * numer_w / (jnp.dot(basis, gram_h, precision=highest, preferred_element_type=jnp.float32) + EPS)
    return basis, profiles
```

```python
import math

import jax
import jax.numpy as jnp
from jax import lax
from jax.sharding import PartitionSpec as P

MZ = 256
MOB = 16
PEAKS = 256
ITERS = 2


EPS = 1e-06


def bin_block(args):
    mass, mobility, weight = args
    mass_hot = (mass[:, :, None] == jnp.arange(MZ, dtype=jnp.int32)[None, None, :]).astype(
        jnp.bfloat16
    ) * weight[:, :, None]
    mobility_hot = (mobility[:, :, None] == jnp.arange(MOB, dtype=jnp.int32)[None, None, :]).astype(
        jnp.bfloat16
    )
    dense = jnp.einsum("pkb,pkm->pbm", mobility_hot, mass_hot, preferred_element_type=jnp.float32)
    return dense.reshape(mass.shape[0], MZ * MOB).astype(jnp.bfloat16)


def pairs(n, s):
    return [(i, i ^ s) for i in range(n)]


def halve_scatter(x, g, axis, n):
    j = lax.axis_index(axis)
    s = n // 2
    while s >= 1:
        half = x.shape[1] // 2
        bit = (j // s) % 2
        keep = lax.dynamic_slice_in_dim(x, bit * half, half, axis=1)
        send = lax.dynamic_slice_in_dim(x, (1 - bit) * half, half, axis=1)
        got = lax.ppermute(jnp.concatenate([send, g], axis=1), axis, pairs(n, s))
        x = keep + got[:, :half]
        g = g + got[:, half:]
        s //= 2
    return x, g


def double_sum(x, axis, n):
    s = 1
    while s < n:
        x = x + lax.ppermute(x, axis, pairs(n, s))
        s *= 2
    return x


def double_gather(x, g, axis, n):
    j = lax.axis_index(axis)
    s = 1
    while s < n:
        other, got_g = lax.ppermute((x, g), axis, pairs(n, s))
        bit = (j // s) % 2
        x = jnp.where(bit == 1, jnp.concatenate([other, x], axis=1), jnp.concatenate([x, other], axis=1))
        g = g + got_g
        s *= 2
    return x, g


def local(mass_bin, mobility_bin, intensity, basis_init, profile_init):
    n_pix = lax.psum(1, "pix")
    n_feat = lax.psum(1, "feat")
    rows = mass_bin.shape[0]
    block = math.gcd(rows, 32)
    count = rows // block
    spectra = lax.map(
        bin_block,
        (
            mass_bin.reshape(count, block, PEAKS),
            mobility_bin.reshape(count, block, PEAKS),
            intensity.reshape(count, block, PEAKS),
        ),
    )
    spectra = spectra.reshape(rows, MZ * MOB)
    highest = lax.Precision.HIGHEST
    basis, profiles = (basis_init, profile_init)
    for step in range(ITERS):
        partial_h = lax.dot_general(
            basis.astype(jnp.bfloat16),
            spectra,
            (((0,), (0,)), ((), ())),
            preferred_element_type=jnp.float32,
        )
        partial_gram = lax.dot_general(
            basis,
            basis,
            (((0,), (0,)), ((), ())),
            precision=highest,
            preferred_element_type=jnp.float32,
        )
        shared, gram_feat = halve_scatter(partial_h, partial_gram, "feat", n_feat)
        both = double_sum(jnp.concatenate([shared, gram_feat], axis=1), "pix", n_pix)
        width = shared.shape[1]
        numer_h = both[:, :width]
        gram_w = both[:, width:]
        profiles = (
            profiles
            * numer_h
            / (
                jnp.dot(gram_w, profiles, precision=highest, preferred_element_type=jnp.float32)
                + EPS
            )
        )
        local_gram = lax.dot_general(
            profiles,
            profiles,
            (((1,), (1,)), ((), ())),
            precision=highest,
            preferred_element_type=jnp.float32,
        )
        profiles_all, gram_h = double_gather(profiles.astype(jnp.bfloat16), local_gram, "feat", n_feat)
        numer_w = lax.dot_general(
            spectra,
            profiles_all,
            (((1,), (1,)), ((), ())),
            preferred_element_type=jnp.float32,
        )
        basis = (
            basis
            * numer_w
            / (jnp.dot(basis, gram_h, precision=highest, preferred_element_type=jnp.float32) + EPS)
        )
    return (basis, profiles)


def solution(mesh):
    return jax.shard_map(
        local,
        mesh=mesh,
        in_specs=(
            P(("pix", "feat"), None),
            P(("pix", "feat"), None),
            P(("pix", "feat"), None),
            P(("pix", "feat"), None),
            P(None, "feat"),
        ),
        out_specs=(P(("pix", "feat"), None), P(None, "feat")),
        check_vma=False,
    )
```

```python
import math

import jax
import jax.numpy as jnp
from jax import lax
from jax.sharding import PartitionSpec as P

MZ = 256
MOB = 16
PEAKS = 256
ITERS = 2
SIDE = 64


EPS = 1e-06


def bin_block(args):
    mass, mobility, weight = args
    feature = mobility * MZ + mass
    hi = feature // SIDE
    lo = feature % SIDE
    side = jnp.arange(SIDE, dtype=jnp.int32)
    hi_hot = (hi[:, :, None] == side[None, None, :]).astype(jnp.bfloat16) * weight[:, :, None]
    lo_hot = (lo[:, :, None] == side[None, None, :]).astype(jnp.bfloat16)
    dense = jnp.einsum("pkh,pkl->phl", hi_hot, lo_hot, preferred_element_type=jnp.float32)
    return dense.reshape(mass.shape[0], MZ * MOB).astype(jnp.bfloat16)


def pairs(n, s):
    return [(i, i ^ s) for i in range(n)]


def halve_scatter(x, g, axis, n):
    j = lax.axis_index(axis)
    s = n // 2
    while s >= 1:
        half = x.shape[1] // 2
        bit = (j // s) % 2
        keep = lax.dynamic_slice_in_dim(x, bit * half, half, axis=1)
        send = lax.dynamic_slice_in_dim(x, (1 - bit) * half, half, axis=1)
        got = lax.ppermute(jnp.concatenate([send, g], axis=1), axis, pairs(n, s))
        x = keep + got[:, :half]
        g = g + got[:, half:]
        s //= 2
    return x, g


def double_sum(x, axis, n):
    s = 1
    while s < n:
        x = x + lax.ppermute(x, axis, pairs(n, s))
        s *= 2
    return x


def double_gather(x, g, axis, n):
    j = lax.axis_index(axis)
    s = 1
    while s < n:
        other, got_g = lax.ppermute((x, g), axis, pairs(n, s))
        bit = (j // s) % 2
        x = jnp.where(bit == 1, jnp.concatenate([other, x], axis=1), jnp.concatenate([x, other], axis=1))
        g = g + got_g
        s *= 2
    return x, g


def local(mass_bin, mobility_bin, intensity, basis_init, profile_init):
    n_pix = lax.psum(1, "pix")
    n_feat = lax.psum(1, "feat")
    rows = mass_bin.shape[0]
    block = math.gcd(rows, 1024)
    count = rows // block
    spectra = lax.map(
        bin_block,
        (
            mass_bin.reshape(count, block, PEAKS),
            mobility_bin.reshape(count, block, PEAKS),
            intensity.reshape(count, block, PEAKS),
        ),
    )
    spectra = spectra.reshape(rows, MZ * MOB)
    highest = lax.Precision.HIGHEST
    basis, profiles = (basis_init, profile_init)
    for step in range(ITERS):
        partial_h = lax.dot_general(
            basis.astype(jnp.bfloat16),
            spectra,
            (((0,), (0,)), ((), ())),
            preferred_element_type=jnp.float32,
        )
        partial_gram = lax.dot_general(
            basis,
            basis,
            (((0,), (0,)), ((), ())),
            precision=highest,
            preferred_element_type=jnp.float32,
        )
        shared, gram_feat = halve_scatter(partial_h, partial_gram, "feat", n_feat)
        both = double_sum(jnp.concatenate([shared, gram_feat], axis=1), "pix", n_pix)
        width = shared.shape[1]
        numer_h = both[:, :width]
        gram_w = both[:, width:]
        profiles = (
            profiles
            * numer_h
            / (
                jnp.dot(gram_w, profiles, precision=highest, preferred_element_type=jnp.float32)
                + EPS
            )
        )
        local_gram = lax.dot_general(
            profiles,
            profiles,
            (((1,), (1,)), ((), ())),
            precision=highest,
            preferred_element_type=jnp.float32,
        )
        profiles_all, gram_h = double_gather(profiles.astype(jnp.bfloat16), local_gram, "feat", n_feat)
        numer_w = lax.dot_general(
            spectra,
            profiles_all,
            (((1,), (1,)), ((), ())),
            preferred_element_type=jnp.float32,
        )
        basis = (
            basis
            * numer_w
            / (jnp.dot(basis, gram_h, precision=highest, preferred_element_type=jnp.float32) + EPS)
        )
    return (basis, profiles)


def solution(mesh):
    return jax.shard_map(
        local,
        mesh=mesh,
        in_specs=(
            P(("pix", "feat"), None),
            P(("pix", "feat"), None),
            P(("pix", "feat"), None),
            P(("pix", "feat"), None),
            P(None, "feat"),
        ),
        out_specs=(P(("pix", "feat"), None), P(None, "feat")),
        check_vma=False,
    )
```

```python
import math

import jax
import jax.numpy as jnp
from jax import lax
from jax.sharding import PartitionSpec as P

MZ = 256
MOB = 16
PEAKS = 256
ITERS = 2
SIDE = 64


EPS = 1e-06


def bin_block(args):
    mass, mobility, weight = args
    feature = mobility * MZ + mass
    hi = feature // SIDE
    lo = feature % SIDE
    side = jnp.arange(SIDE, dtype=jnp.int32)
    hi_hot = (hi[:, :, None] == side[None, None, :]).astype(jnp.bfloat16) * weight[:, :, None]
    lo_hot = (lo[:, :, None] == side[None, None, :]).astype(jnp.bfloat16)
    dense = jnp.einsum("pkh,pkl->phl", hi_hot, lo_hot, preferred_element_type=jnp.float32)
    return dense.reshape(mass.shape[0], MZ * MOB).astype(jnp.bfloat16)


def pairs(n, s):
    return [(i, i ^ s) for i in range(n)]


def scatter_once(x, g, axis, n):
    j = lax.axis_index(axis)
    w = x.shape[1] // n
    acc = jnp.concatenate([lax.dynamic_slice_in_dim(x, j * w, w, axis=1), g], axis=1)
    for t in range(1, n):
        send = jnp.concatenate([lax.dynamic_slice_in_dim(x, ((j + t) % n) * w, w, axis=1), g], axis=1)
        acc = acc + lax.ppermute(send, axis, [(i, (i + t) % n) for i in range(n)])
    return acc[:, :w], acc[:, w:]


def halve_sum(x, axis, n):
    j = lax.axis_index(axis)
    half = x.shape[1] // 2
    bit = j % 2
    keep = lax.dynamic_slice_in_dim(x, bit * half, half, axis=1)
    send = lax.dynamic_slice_in_dim(x, (1 - bit) * half, half, axis=1)
    x = keep + lax.ppermute(send, axis, pairs(n, 1))
    s = 2
    while s < n:
        x = x + lax.ppermute(x, axis, pairs(n, s))
        s *= 2
    other = lax.ppermute(x, axis, pairs(n, 1))
    return jnp.where(bit == 1, jnp.concatenate([other, x], axis=1), jnp.concatenate([x, other], axis=1))


def double_gather(x, g, axis, n):
    j = lax.axis_index(axis)
    s = 1
    while s < n:
        other, got_g = lax.ppermute((x, g), axis, pairs(n, s))
        bit = (j // s) % 2
        x = jnp.where(bit == 1, jnp.concatenate([other, x], axis=1), jnp.concatenate([x, other], axis=1))
        g = g + got_g
        s *= 2
    return x, g


def local(mass_bin, mobility_bin, intensity, basis_init, profile_init):
    n_pix = lax.psum(1, "pix")
    n_feat = lax.psum(1, "feat")
    rows = mass_bin.shape[0]
    block = math.gcd(rows, 1024)
    count = rows // block
    spectra = lax.map(
        bin_block,
        (
            mass_bin.reshape(count, block, PEAKS),
            mobility_bin.reshape(count, block, PEAKS),
            intensity.reshape(count, block, PEAKS),
        ),
    )
    spectra = spectra.reshape(rows, MZ * MOB)
    highest = lax.Precision.HIGHEST
    basis, profiles = (basis_init, profile_init)
    def round_(step, carry):
        basis, profiles = carry
        partial_h = lax.dot_general(
            basis.astype(jnp.bfloat16),
            spectra,
            (((0,), (0,)), ((), ())),
            preferred_element_type=jnp.float32,
        )
        partial_gram = lax.dot_general(
            basis,
            basis,
            (((0,), (0,)), ((), ())),
            precision=highest,
            preferred_element_type=jnp.float32,
        )
        shared, gram_feat = scatter_once(partial_h, partial_gram, "feat", n_feat)
        both = halve_sum(jnp.concatenate([shared, gram_feat], axis=1), "pix", n_pix)
        width = shared.shape[1]
        numer_h = both[:, :width]
        gram_w = both[:, width:]
        profiles = (
            profiles
            * numer_h
            / (
                jnp.dot(gram_w, profiles, precision=highest, preferred_element_type=jnp.float32)
                + EPS
            )
        )
        local_gram = lax.dot_general(
            profiles,
            profiles,
            (((1,), (1,)), ((), ())),
            precision=highest,
            preferred_element_type=jnp.float32,
        )
        profiles_all, gram_h = double_gather(profiles.astype(jnp.bfloat16), local_gram, "feat", n_feat)
        numer_w = lax.dot_general(
            spectra,
            profiles_all,
            (((1,), (1,)), ((), ())),
            preferred_element_type=jnp.float32,
        )
        basis = (
            basis
            * numer_w
            / (jnp.dot(basis, gram_h, precision=highest, preferred_element_type=jnp.float32) + EPS)
        )
        return (basis, profiles)

    basis, profiles = lax.fori_loop(0, ITERS, round_, (basis, profiles))
    return (basis, profiles)


def solution(mesh):
    return jax.shard_map(
        local,
        mesh=mesh,
        in_specs=(
            P(("pix", "feat"), None),
            P(("pix", "feat"), None),
            P(("pix", "feat"), None),
            P(("pix", "feat"), None),
            P(None, "feat"),
        ),
        out_specs=(P(("pix", "feat"), None), P(None, "feat")),
        check_vma=False,
    )
```

```python
import math

import jax
import jax.numpy as jnp
from jax import lax
from jax.sharding import PartitionSpec as P

MZ = 256
MOB = 16
PEAKS = 256
ITERS = 2
SIDE = 64


EPS = 1e-06


def bin_block(args):
    mass, mobility, weight = args
    feature = mobility * MZ + mass
    hi = feature // SIDE
    lo = feature % SIDE
    side = jnp.arange(SIDE, dtype=jnp.int32)
    hi_hot = (hi[:, :, None] == side[None, None, :]).astype(jnp.bfloat16) * weight[:, :, None]
    lo_hot = (lo[:, :, None] == side[None, None, :]).astype(jnp.bfloat16)
    dense = jnp.einsum("pkh,pkl->phl", hi_hot, lo_hot, preferred_element_type=jnp.float32)
    return dense.reshape(mass.shape[0], MZ * MOB).astype(jnp.bfloat16)


def pairs(n, s):
    return [(i, i ^ s) for i in range(n)]


def scatter_once(x, g, axis, n):
    j = lax.axis_index(axis)
    w = x.shape[1] // n
    x = jnp.roll(x, -j * w, axis=1)
    acc = jnp.concatenate([x[:, :w], g], axis=1)
    for t in range(1, n):
        send = jnp.concatenate([x[:, t * w : (t + 1) * w], g], axis=1)
        acc = acc + lax.ppermute(send, axis, [(i, (i + t) % n) for i in range(n)])
    return acc[:, :w], acc[:, w:]


def halve_sum(x, axis, n):
    j = lax.axis_index(axis)
    half = x.shape[1] // 2
    bit = j % 2
    keep = lax.dynamic_slice_in_dim(x, bit * half, half, axis=1)
    send = lax.dynamic_slice_in_dim(x, (1 - bit) * half, half, axis=1)
    x = keep + lax.ppermute(send, axis, pairs(n, 1))
    s = 2
    while s < n:
        x = x + lax.ppermute(x, axis, pairs(n, s))
        s *= 2
    other = lax.ppermute(x, axis, pairs(n, 1))
    return jnp.where(bit == 1, jnp.concatenate([other, x], axis=1), jnp.concatenate([x, other], axis=1))


def double_gather(x, g, axis, n):
    j = lax.axis_index(axis)
    s = 1
    while s < n:
        other, got_g = lax.ppermute((x, g), axis, pairs(n, s))
        bit = (j // s) % 2
        x = jnp.where(bit == 1, jnp.concatenate([other, x], axis=1), jnp.concatenate([x, other], axis=1))
        g = g + got_g
        s *= 2
    return x, g


def local(mass_bin, mobility_bin, intensity, basis_init, profile_init):
    n_pix = lax.psum(1, "pix")
    n_feat = lax.psum(1, "feat")
    rows = mass_bin.shape[0]
    block = math.gcd(rows, 1024)
    count = rows // block
    spectra = lax.map(
        bin_block,
        (
            mass_bin.reshape(count, block, PEAKS),
            mobility_bin.reshape(count, block, PEAKS),
            intensity.reshape(count, block, PEAKS),
        ),
    )
    spectra = spectra.reshape(rows, MZ * MOB)
    highest = lax.Precision.HIGHEST
    basis, profiles = (basis_init, profile_init)
    for step in range(ITERS):
        partial_h = lax.dot_general(
            basis.astype(jnp.bfloat16),
            spectra,
            (((0,), (0,)), ((), ())),
            preferred_element_type=jnp.float32,
        )
        partial_gram = lax.dot_general(
            basis,
            basis,
            (((0,), (0,)), ((), ())),
            precision=highest,
            preferred_element_type=jnp.float32,
        )
        shared, gram_feat = scatter_once(partial_h, partial_gram, "feat", n_feat)
        both = halve_sum(jnp.concatenate([shared, gram_feat], axis=1), "pix", n_pix)
        width = shared.shape[1]
        numer_h = both[:, :width]
        gram_w = both[:, width:]
        profiles = (
            profiles
            * numer_h
            / (
                jnp.dot(gram_w, profiles, precision=highest, preferred_element_type=jnp.float32)
                + EPS
            )
        )
        local_gram = lax.dot_general(
            profiles,
            profiles,
            (((1,), (1,)), ((), ())),
            precision=highest,
            preferred_element_type=jnp.float32,
        )
        profiles_all, gram_h = double_gather(profiles.astype(jnp.bfloat16), local_gram, "feat", n_feat)
        numer_w = lax.dot_general(
            spectra,
            profiles_all,
            (((1,), (1,)), ((), ())),
            preferred_element_type=jnp.float32,
        )
        basis = (
            basis
            * numer_w
            / (jnp.dot(basis, gram_h, precision=highest, preferred_element_type=jnp.float32) + EPS)
        )
    return (basis, profiles)


def solution(mesh):
    return jax.shard_map(
        local,
        mesh=mesh,
        in_specs=(
            P(("pix", "feat"), None),
            P(("pix", "feat"), None),
            P(("pix", "feat"), None),
            P(("pix", "feat"), None),
            P(None, "feat"),
        ),
        out_specs=(P(("pix", "feat"), None), P(None, "feat")),
        check_vma=False,
    )
```

```python
import math

import jax
import jax.numpy as jnp
from jax import lax
from jax.sharding import PartitionSpec as P

MZ = 256
MOB = 16
PEAKS = 256
ITERS = 2
SIDE = 64


EPS = 1e-06


def bin_block(args):
    mass, mobility, weight = args
    feature = mobility * MZ + mass
    hi = feature // SIDE
    lo = feature % SIDE
    side = jnp.arange(SIDE, dtype=jnp.int32)
    hi_hot = (hi[:, :, None] == side[None, None, :]).astype(jnp.bfloat16) * weight[:, :, None]
    lo_hot = (lo[:, :, None] == side[None, None, :]).astype(jnp.bfloat16)
    dense = jnp.einsum("pkh,pkl->phl", hi_hot, lo_hot, preferred_element_type=jnp.float32)
    return dense.reshape(mass.shape[0], MZ * MOB).astype(jnp.bfloat16)


def pairs(n, s):
    return [(i, i ^ s) for i in range(n)]


def scatter_once(x, g, axis, n):
    j = lax.axis_index(axis)
    w = x.shape[1] // n
    x = jnp.roll(x, -j * w, axis=1)
    acc = jnp.concatenate([x[:, :w], g], axis=1)
    for t in range(1, n):
        send = jnp.concatenate([x[:, t * w : (t + 1) * w], g], axis=1)
        acc = acc + lax.ppermute(send, axis, [(i, (i + t) % n) for i in range(n)])
    return acc[:, :w], acc[:, w:]


CORE_BITS = ((0, 2, 3, 4, 1), (2, 0, 1, 3, 4))


def core_pairs(n_pix, n_feat, s):
    out = []
    for d in range(n_pix * n_feat):
        p, f = divmod(d, n_feat)
        bit = CORE_BITS[f % 2][s]
        out.append((d, (p ^ (1 << bit)) * n_feat + f))
    return out


def halve_sum(x, n_pix, n_feat):
    axes = ("pix", "feat")
    p = lax.axis_index("pix")
    core = lax.axis_index("feat") % 2
    first = jnp.where(core == 0, 1 << CORE_BITS[0][0], 1 << CORE_BITS[1][0])
    half = x.shape[1] // 2
    bit = (p // first) % 2
    keep = lax.dynamic_slice_in_dim(x, bit * half, half, axis=1)
    send = lax.dynamic_slice_in_dim(x, (1 - bit) * half, half, axis=1)
    x = keep + lax.ppermute(send, axes, core_pairs(n_pix, n_feat, 0))
    for s in range(1, len(CORE_BITS[0])):
        x = x + lax.ppermute(x, axes, core_pairs(n_pix, n_feat, s))
    other = lax.ppermute(x, axes, core_pairs(n_pix, n_feat, 0))
    return jnp.where(bit == 1, jnp.concatenate([other, x], axis=1), jnp.concatenate([x, other], axis=1))


def double_gather(x, g, axis, n):
    j = lax.axis_index(axis)
    s = 1
    while s < n:
        other, got_g = lax.ppermute((x, g), axis, pairs(n, s))
        bit = (j // s) % 2
        x = jnp.where(bit == 1, jnp.concatenate([other, x], axis=1), jnp.concatenate([x, other], axis=1))
        g = g + got_g
        s *= 2
    return x, g


def local(mass_bin, mobility_bin, intensity, basis_init, profile_init):
    n_pix = lax.psum(1, "pix")
    n_feat = lax.psum(1, "feat")
    rows = mass_bin.shape[0]
    block = math.gcd(rows, 1024)
    count = rows // block
    spectra = lax.map(
        bin_block,
        (
            mass_bin.reshape(count, block, PEAKS),
            mobility_bin.reshape(count, block, PEAKS),
            intensity.reshape(count, block, PEAKS),
        ),
    )
    spectra = spectra.reshape(rows, MZ * MOB)
    highest = lax.Precision.HIGHEST
    basis, profiles = (basis_init, profile_init)
    for step in range(ITERS):
        partial_h = lax.dot_general(
            basis.astype(jnp.bfloat16),
            spectra,
            (((0,), (0,)), ((), ())),
            preferred_element_type=jnp.float32,
        )
        partial_gram = lax.dot_general(
            basis,
            basis,
            (((0,), (0,)), ((), ())),
            precision=highest,
            preferred_element_type=jnp.float32,
        )
        shared, gram_feat = scatter_once(partial_h, partial_gram, "feat", n_feat)
        both = halve_sum(jnp.concatenate([shared, gram_feat], axis=1), n_pix, n_feat)
        width = shared.shape[1]
        numer_h = both[:, :width]
        gram_w = both[:, width:]
        profiles = (
            profiles
            * numer_h
            / (
                jnp.dot(gram_w, profiles, precision=highest, preferred_element_type=jnp.float32)
                + EPS
            )
        )
        local_gram = lax.dot_general(
            profiles,
            profiles,
            (((1,), (1,)), ((), ())),
            precision=highest,
            preferred_element_type=jnp.float32,
        )
        profiles_all, gram_h = double_gather(profiles.astype(jnp.bfloat16), local_gram, "feat", n_feat)
        numer_w = lax.dot_general(
            spectra,
            profiles_all,
            (((1,), (1,)), ((), ())),
            preferred_element_type=jnp.float32,
        )
        basis = (
            basis
            * numer_w
            / (jnp.dot(basis, gram_h, precision=highest, preferred_element_type=jnp.float32) + EPS)
        )
    return (basis, profiles)


def solution(mesh):
    return jax.shard_map(
        local,
        mesh=mesh,
        in_specs=(
            P(("pix", "feat"), None),
            P(("pix", "feat"), None),
            P(("pix", "feat"), None),
            P(("pix", "feat"), None),
            P(None, "feat"),
        ),
        out_specs=(P(("pix", "feat"), None), P(None, "feat")),
        check_vma=False,
    )
```

```python
import math

import jax
import jax.numpy as jnp
from jax import lax
from jax.sharding import PartitionSpec as P

MZ = 256
MOB = 16
PEAKS = 256
ITERS = 2
SIDE = 64


EPS = 1e-06


def bin_block(args):
    mass, mobility, weight = args
    feature = mobility * MZ + mass
    hi = feature // SIDE
    lo = feature % SIDE
    side = jnp.arange(SIDE, dtype=jnp.int32)
    hi_hot = (hi[:, :, None] == side[None, None, :]).astype(jnp.bfloat16) * weight[:, :, None]
    lo_hot = (lo[:, :, None] == side[None, None, :]).astype(jnp.bfloat16)
    dense = jnp.einsum("pkh,pkl->phl", hi_hot, lo_hot, preferred_element_type=jnp.float32)
    return dense.reshape(mass.shape[0], MZ * MOB).astype(jnp.bfloat16)


def pairs(n, s):
    return [(i, i ^ s) for i in range(n)]


def scatter_once(x, g, axis, n):
    j = lax.axis_index(axis)
    w = x.shape[1] // n
    x = jnp.roll(x, -j * w, axis=1)
    acc = jnp.concatenate([x[:, :w], g], axis=1)
    for t in range(1, n):
        send = jnp.concatenate([x[:, t * w : (t + 1) * w], g], axis=1)
        acc = acc + lax.ppermute(send, axis, [(i, (i + t) % n) for i in range(n)])
    return acc[:, :w], acc[:, w:]


CORE_BITS = ((0, 2, 3, 4, 1), (2, 0, 1, 3, 4))


def core_pairs(n_pix, n_feat, s):
    out = []
    for d in range(n_pix * n_feat):
        p, f = divmod(d, n_feat)
        bit = CORE_BITS[f % 2][s]
        out.append((d, (p ^ (1 << bit)) * n_feat + f))
    return out


def halve_sum(x, n_pix, n_feat):
    axes = ("pix", "feat")
    p = lax.axis_index("pix")
    core = lax.axis_index("feat") % 2
    first = jnp.where(core == 0, 1 << CORE_BITS[0][0], 1 << CORE_BITS[1][0])
    half = x.shape[1] // 2
    bit = (p // first) % 2
    keep = lax.dynamic_slice_in_dim(x, bit * half, half, axis=1)
    send = lax.dynamic_slice_in_dim(x, (1 - bit) * half, half, axis=1)
    x = keep + lax.ppermute(send, axes, core_pairs(n_pix, n_feat, 0))
    for s in range(1, len(CORE_BITS[0])):
        x = x + lax.ppermute(x, axes, core_pairs(n_pix, n_feat, s))
    other = lax.ppermute(x, axes, core_pairs(n_pix, n_feat, 0))
    return jnp.where(bit == 1, jnp.concatenate([other, x], axis=1), jnp.concatenate([x, other], axis=1))


def exchange_gather(x, g, axis, n):
    xs = lax.all_to_all(jnp.broadcast_to(x[None], (n,) + x.shape), axis, 0, 0, tiled=True)
    gs = lax.all_to_all(jnp.broadcast_to(g[None], (n,) + g.shape), axis, 0, 0, tiled=True)
    total = gs[0]
    for t in range(1, n):
        total = total + gs[t]
    return xs.transpose(1, 0, 2).reshape(x.shape[0], n * x.shape[1]), total


def local(mass_bin, mobility_bin, intensity, basis_init, profile_init):
    n_pix = lax.psum(1, "pix")
    n_feat = lax.psum(1, "feat")
    rows = mass_bin.shape[0]
    block = math.gcd(rows, 1024)
    count = rows // block
    spectra = lax.map(
        bin_block,
        (
            mass_bin.reshape(count, block, PEAKS),
            mobility_bin.reshape(count, block, PEAKS),
            intensity.reshape(count, block, PEAKS),
        ),
    )
    spectra = spectra.reshape(rows, MZ * MOB)
    highest = lax.Precision.HIGHEST
    basis, profiles = (basis_init, profile_init)
    for step in range(ITERS):
        partial_h = lax.dot_general(
            basis.astype(jnp.bfloat16),
            spectra,
            (((0,), (0,)), ((), ())),
            preferred_element_type=jnp.float32,
        )
        partial_gram = lax.dot_general(
            basis,
            basis,
            (((0,), (0,)), ((), ())),
            precision=highest,
            preferred_element_type=jnp.float32,
        )
        shared, gram_feat = scatter_once(partial_h, partial_gram, "feat", n_feat)
        both = halve_sum(jnp.concatenate([shared, gram_feat], axis=1), n_pix, n_feat)
        width = shared.shape[1]
        numer_h = both[:, :width]
        gram_w = both[:, width:]
        profiles = (
            profiles
            * numer_h
            / (
                jnp.dot(gram_w, profiles, precision=highest, preferred_element_type=jnp.float32)
                + EPS
            )
        )
        local_gram = lax.dot_general(
            profiles,
            profiles,
            (((1,), (1,)), ((), ())),
            precision=highest,
            preferred_element_type=jnp.float32,
        )
        profiles_all, gram_h = exchange_gather(profiles.astype(jnp.bfloat16), local_gram, "feat", n_feat)
        numer_w = lax.dot_general(
            spectra,
            profiles_all,
            (((1,), (1,)), ((), ())),
            preferred_element_type=jnp.float32,
        )
        basis = (
            basis
            * numer_w
            / (jnp.dot(basis, gram_h, precision=highest, preferred_element_type=jnp.float32) + EPS)
        )
    return (basis, profiles)


def solution(mesh):
    return jax.shard_map(
        local,
        mesh=mesh,
        in_specs=(
            P(("pix", "feat"), None),
            P(("pix", "feat"), None),
            P(("pix", "feat"), None),
            P(("pix", "feat"), None),
            P(None, "feat"),
        ),
        out_specs=(P(("pix", "feat"), None), P(None, "feat")),
        check_vma=False,
    )
```

```python
import math

import jax
import jax.numpy as jnp
from jax import lax
from jax.sharding import PartitionSpec as P

MZ = 256
MOB = 16
PEAKS = 256
ITERS = 2
SIDE = 64


EPS = 1e-06


def bin_block(args):
    mass, mobility, weight = args
    feature = mobility * MZ + mass
    hi = feature // SIDE
    lo = feature % SIDE
    side = jnp.arange(SIDE, dtype=jnp.int32)
    hi_hot = (hi[:, :, None] == side[None, None, :]).astype(jnp.bfloat16) * weight[:, :, None]
    lo_hot = (lo[:, :, None] == side[None, None, :]).astype(jnp.bfloat16)
    dense = jnp.einsum("pkh,pkl->phl", hi_hot, lo_hot, preferred_element_type=jnp.float32)
    return dense.reshape(mass.shape[0], MZ * MOB).astype(jnp.bfloat16)


def pairs(n, s):
    return [(i, i ^ s) for i in range(n)]


def scatter_once(block_of, g, axis, n):
    j = lax.axis_index(axis)
    acc = jnp.concatenate([block_of(j), g], axis=1)
    for t in range(1, n):
        send = jnp.concatenate([block_of((j + t) % n), g], axis=1)
        acc = acc + lax.ppermute(send, axis, [(i, (i + t) % n) for i in range(n)])
    w = acc.shape[1] - g.shape[1]
    return acc[:, :w], acc[:, w:]


CORE_BITS = ((0, 2, 3, 4, 1), (2, 0, 1, 3, 4))


def core_pairs(n_pix, n_feat, s):
    out = []
    for d in range(n_pix * n_feat):
        p, f = divmod(d, n_feat)
        bit = CORE_BITS[f % 2][s]
        out.append((d, (p ^ (1 << bit)) * n_feat + f))
    return out


def halve_sum(x, n_pix, n_feat):
    axes = ("pix", "feat")
    p = lax.axis_index("pix")
    core = lax.axis_index("feat") % 2
    first = jnp.where(core == 0, 1 << CORE_BITS[0][0], 1 << CORE_BITS[1][0])
    half = x.shape[1] // 2
    bit = (p // first) % 2
    keep = lax.dynamic_slice_in_dim(x, bit * half, half, axis=1)
    send = lax.dynamic_slice_in_dim(x, (1 - bit) * half, half, axis=1)
    x = keep + lax.ppermute(send, axes, core_pairs(n_pix, n_feat, 0))
    for s in range(1, len(CORE_BITS[0])):
        x = x + lax.ppermute(x, axes, core_pairs(n_pix, n_feat, s))
    other = lax.ppermute(x, axes, core_pairs(n_pix, n_feat, 0))
    return jnp.where(bit == 1, jnp.concatenate([other, x], axis=1), jnp.concatenate([x, other], axis=1))


def double_gather(x, g, use, axis, n):
    j = lax.axis_index(axis)
    out = use(j, x)
    s = 1
    while s < n:
        other, got_g = lax.ppermute((x, g), axis, pairs(n, s))
        bit = (j // s) % 2
        out = out + use((j // s ^ 1) * s, other)
        x = jnp.where(bit == 1, jnp.concatenate([other, x], axis=1), jnp.concatenate([x, other], axis=1))
        g = g + got_g
        s *= 2
    return out, g


def local(mass_bin, mobility_bin, intensity, basis_init, profile_init):
    n_pix = lax.psum(1, "pix")
    n_feat = lax.psum(1, "feat")
    rows = mass_bin.shape[0]
    block = math.gcd(rows, 1024)
    count = rows // block
    spectra = lax.map(
        bin_block,
        (
            mass_bin.reshape(count, block, PEAKS),
            mobility_bin.reshape(count, block, PEAKS),
            intensity.reshape(count, block, PEAKS),
        ),
    )
    spectra = spectra.reshape(rows, MZ * MOB)
    highest = lax.Precision.HIGHEST
    basis, profiles = (basis_init, profile_init)
    for step in range(ITERS):
        basis_b = basis.astype(jnp.bfloat16)
        width = spectra.shape[1] // n_feat

        def numer_h_block(b, basis_b=basis_b, width=width):
            return lax.dot_general(
                basis_b,
                lax.dynamic_slice_in_dim(spectra, b * width, width, axis=1),
                (((0,), (0,)), ((), ())),
                preferred_element_type=jnp.float32,
            )

        partial_gram = lax.dot_general(
            basis,
            basis,
            (((0,), (0,)), ((), ())),
            precision=highest,
            preferred_element_type=jnp.float32,
        )
        shared, gram_feat = scatter_once(numer_h_block, partial_gram, "feat", n_feat)
        both = halve_sum(jnp.concatenate([shared, gram_feat], axis=1), n_pix, n_feat)
        numer_h = both[:, :width]
        gram_w = both[:, width:]
        profiles = (
            profiles
            * numer_h
            / (
                jnp.dot(gram_w, profiles, precision=highest, preferred_element_type=jnp.float32)
                + EPS
            )
        )
        local_gram = lax.dot_general(
            profiles,
            profiles,
            (((1,), (1,)), ((), ())),
            precision=highest,
            preferred_element_type=jnp.float32,
        )

        def numer_w_part(first, blocks, width=width):
            return lax.dot_general(
                lax.dynamic_slice_in_dim(spectra, first * width, blocks.shape[1], axis=1),
                blocks,
                (((1,), (1,)), ((), ())),
                preferred_element_type=jnp.float32,
            )

        numer_w, gram_h = double_gather(profiles.astype(jnp.bfloat16), local_gram, numer_w_part, "feat", n_feat)
        basis = (
            basis
            * numer_w
            / (jnp.dot(basis, gram_h, precision=highest, preferred_element_type=jnp.float32) + EPS)
        )
    return (basis, profiles)


def solution(mesh):
    return jax.shard_map(
        local,
        mesh=mesh,
        in_specs=(
            P(("pix", "feat"), None),
            P(("pix", "feat"), None),
            P(("pix", "feat"), None),
            P(("pix", "feat"), None),
            P(None, "feat"),
        ),
        out_specs=(P(("pix", "feat"), None), P(None, "feat")),
        check_vma=False,
    )
```

```python
import math

import jax
import jax.numpy as jnp
from jax import lax
from jax.sharding import PartitionSpec as P

MZ = 256
MOB = 16
PEAKS = 256
ITERS = 2
SIDE = 64


EPS = 1e-06


def bin_block(args):
    mass, mobility, weight = args
    feature = mobility * MZ + mass
    hi = feature >> 6
    lo = feature & (SIDE - 1)
    side = jnp.arange(SIDE, dtype=jnp.int32)
    hi_hot = (hi[:, :, None] == side[None, None, :]).astype(jnp.bfloat16) * weight[:, :, None]
    lo_hot = (lo[:, :, None] == side[None, None, :]).astype(jnp.bfloat16)
    dense = jnp.einsum("pkh,pkl->phl", hi_hot, lo_hot, preferred_element_type=jnp.float32)
    return dense.reshape(mass.shape[0], MZ * MOB).astype(jnp.bfloat16)


def pairs(n, s):
    return [(i, i ^ s) for i in range(n)]


def scatter_once(x, g, axis, n):
    j = lax.axis_index(axis)
    core = j % 2
    y = j // 2
    w = x.shape[1] // n
    rows = x.shape[0]
    x = x.reshape(rows, n // 2, 2, w)
    keep = lax.dynamic_index_in_dim(x, core, axis=2, keepdims=False)
    send = lax.dynamic_index_in_dim(x, 1 - core, axis=2, keepdims=False).reshape(rows, (n // 2) * w)
    got = lax.ppermute(jnp.concatenate([send, g], axis=1), axis, pairs(n, 1))
    half = keep + got[:, : (n // 2) * w].reshape(rows, n // 2, w)
    g = g + got[:, (n // 2) * w :]
    half = jnp.roll(half, -y, axis=1)
    acc = jnp.concatenate([half[:, 0], g], axis=1)
    for t in range(1, n // 2):
        msg = jnp.concatenate([half[:, t], g], axis=1)
        acc = acc + lax.ppermute(msg, axis, [(i, (i + 2 * t) % n) for i in range(n)])
    return acc[:, :w], acc[:, w:]


CORE_BITS = ((0, 2, 3, 4, 1), (2, 0, 1, 3, 4))


def core_pairs(n_pix, n_feat, s):
    out = []
    for d in range(n_pix * n_feat):
        p, f = divmod(d, n_feat)
        bit = CORE_BITS[f % 2][s]
        out.append((d, (p ^ (1 << bit)) * n_feat + f))
    return out


def halve_sum(x, n_pix, n_feat):
    axes = ("pix", "feat")
    p = lax.axis_index("pix")
    core = lax.axis_index("feat") % 2
    first = jnp.where(core == 0, 1 << CORE_BITS[0][0], 1 << CORE_BITS[1][0])
    half = x.shape[1] // 2
    bit = (p // first) % 2
    keep = lax.dynamic_slice_in_dim(x, bit * half, half, axis=1)
    send = lax.dynamic_slice_in_dim(x, (1 - bit) * half, half, axis=1)
    x = keep + lax.ppermute(send, axes, core_pairs(n_pix, n_feat, 0))
    for s in range(1, len(CORE_BITS[0])):
        x = x + lax.ppermute(x, axes, core_pairs(n_pix, n_feat, s))
    other = lax.ppermute(x, axes, core_pairs(n_pix, n_feat, 0))
    return jnp.where(bit == 1, jnp.concatenate([other, x], axis=1), jnp.concatenate([x, other], axis=1))


def double_gather(x, g, axis, n):
    j = lax.axis_index(axis)
    s = 1
    while s < n:
        other, got_g = lax.ppermute((x, g), axis, pairs(n, s))
        bit = (j // s) % 2
        x = jnp.where(bit == 1, jnp.concatenate([other, x], axis=1), jnp.concatenate([x, other], axis=1))
        g = g + got_g
        s *= 2
    return x, g


def local(mass_bin, mobility_bin, intensity, basis_init, profile_init):
    n_pix = lax.psum(1, "pix")
    n_feat = lax.psum(1, "feat")
    rows = mass_bin.shape[0]
    block = math.gcd(rows, 1024)
    count = rows // block
    spectra = lax.map(
        bin_block,
        (
            mass_bin.reshape(count, block, PEAKS),
            mobility_bin.reshape(count, block, PEAKS),
            intensity.reshape(count, block, PEAKS),
        ),
    )
    spectra = spectra.reshape(rows, MZ * MOB)
    highest = lax.Precision.HIGHEST
    basis, profiles = (basis_init, profile_init)
    for step in range(ITERS):
        partial_h = lax.dot_general(
            basis.astype(jnp.bfloat16),
            spectra,
            (((0,), (0,)), ((), ())),
            preferred_element_type=jnp.float32,
        )
        partial_gram = lax.dot_general(
            basis,
            basis,
            (((0,), (0,)), ((), ())),
            precision=highest,
            preferred_element_type=jnp.float32,
        )
        shared, gram_feat = scatter_once(partial_h, partial_gram, "feat", n_feat)
        both = halve_sum(jnp.concatenate([shared, gram_feat], axis=1), n_pix, n_feat)
        width = shared.shape[1]
        numer_h = both[:, :width]
        gram_w = both[:, width:]
        profiles = (
            profiles
            * numer_h
            / (
                jnp.dot(gram_w, profiles, precision=highest, preferred_element_type=jnp.float32)
                + EPS
            )
        )
        local_gram = lax.dot_general(
            profiles,
            profiles,
            (((1,), (1,)), ((), ())),
            precision=highest,
            preferred_element_type=jnp.float32,
        )
        profiles_all, gram_h = double_gather(profiles.astype(jnp.bfloat16), local_gram, "feat", n_feat)
        numer_w = lax.dot_general(
            spectra,
            profiles_all,
            (((1,), (1,)), ((), ())),
            preferred_element_type=jnp.float32,
        )
        basis = (
            basis
            * numer_w
            / (jnp.dot(basis, gram_h, precision=highest, preferred_element_type=jnp.float32) + EPS)
        )
    return (basis, profiles)


def solution(mesh):
    return jax.shard_map(
        local,
        mesh=mesh,
        in_specs=(
            P(("pix", "feat"), None),
            P(("pix", "feat"), None),
            P(("pix", "feat"), None),
            P(("pix", "feat"), None),
            P(None, "feat"),
        ),
        out_specs=(P(("pix", "feat"), None), P(None, "feat")),
        check_vma=False,
    )
```

```python
import math

import jax
import jax.numpy as jnp
from jax import lax
from jax.sharding import PartitionSpec as P

MZ = 256
MOB = 16
PEAKS = 256
ITERS = 2
SIDE = 64


EPS = 1e-06


def bin_block(args):
    mass, mobility, weight = args
    feature = mobility * MZ + mass
    hi = feature // SIDE
    lo = feature % SIDE
    side = jnp.arange(SIDE, dtype=jnp.int32)
    hi_hot = (hi[:, :, None] == side[None, None, :]).astype(jnp.bfloat16) * weight[:, :, None]
    lo_hot = (lo[:, :, None] == side[None, None, :]).astype(jnp.bfloat16)
    dense = jnp.einsum("pkh,pkl->phl", hi_hot, lo_hot, preferred_element_type=jnp.float32)
    return dense.reshape(mass.shape[0], MZ * MOB).astype(jnp.bfloat16)


def pairs(n, s):
    return [(i, i ^ s) for i in range(n)]


def scatter_once(x, g, axis, n):
    j = lax.axis_index(axis)
    w = x.shape[1] // n
    x = jnp.roll(x, -j * w, axis=1)
    acc = jnp.concatenate([x[:, :w], g], axis=1)
    for t in range(1, n):
        send = jnp.concatenate([x[:, t * w : (t + 1) * w], g], axis=1)
        acc = acc + lax.ppermute(send, axis, [(i, (i + t) % n) for i in range(n)])
    return acc[:, :w], acc[:, w:]


CORE_BITS = ((0, 2, 3, 4, 1), (2, 0, 1, 3, 4))


def core_pairs(n_pix, n_feat, s):
    out = []
    for d in range(n_pix * n_feat):
        p, f = divmod(d, n_feat)
        bit = CORE_BITS[f % 2][s]
        out.append((d, (p ^ (1 << bit)) * n_feat + f))
    return out


def halve_sum(x, n_pix, n_feat):
    axes = ("pix", "feat")
    p = lax.axis_index("pix")
    core = lax.axis_index("feat") % 2
    first = jnp.where(core == 0, 1 << CORE_BITS[0][0], 1 << CORE_BITS[1][0])
    half = x.shape[1] // 2
    bit = (p // first) % 2
    keep = lax.dynamic_slice_in_dim(x, bit * half, half, axis=1)
    send = lax.dynamic_slice_in_dim(x, (1 - bit) * half, half, axis=1)
    x = keep + lax.ppermute(send, axes, core_pairs(n_pix, n_feat, 0))
    for s in range(1, len(CORE_BITS[0])):
        x = x + lax.ppermute(x, axes, core_pairs(n_pix, n_feat, s))
    other = lax.ppermute(x, axes, core_pairs(n_pix, n_feat, 0))
    return jnp.where(bit == 1, jnp.concatenate([other, x], axis=1), jnp.concatenate([x, other], axis=1))


def split3(g):
    hi = g.astype(jnp.bfloat16)
    rest = g - hi.astype(jnp.float32)
    mid = rest.astype(jnp.bfloat16)
    lo = (rest - mid.astype(jnp.float32)).astype(jnp.bfloat16)
    return jnp.concatenate([hi, mid, lo], axis=1)


def join3(parts):
    k = parts.shape[1] // 3
    f = parts.astype(jnp.float32)
    return (f[:, :k] + f[:, k : 2 * k]) + f[:, 2 * k :]


def double_gather(x, g, axis, n):
    j = lax.axis_index(axis)
    s = 1
    while s < n:
        w = x.shape[1]
        got = lax.ppermute(jnp.concatenate([x, split3(g)], axis=1), axis, pairs(n, s))
        other = got[:, :w]
        bit = (j // s) % 2
        x = jnp.where(bit == 1, jnp.concatenate([other, x], axis=1), jnp.concatenate([x, other], axis=1))
        g = g + join3(got[:, w:])
        s *= 2
    return x, g


def local(mass_bin, mobility_bin, intensity, basis_init, profile_init):
    n_pix = lax.psum(1, "pix")
    n_feat = lax.psum(1, "feat")
    rows = mass_bin.shape[0]
    block = math.gcd(rows, 1024)
    count = rows // block
    spectra = lax.map(
        bin_block,
        (
            mass_bin.reshape(count, block, PEAKS),
            mobility_bin.reshape(count, block, PEAKS),
            intensity.reshape(count, block, PEAKS),
        ),
    )
    spectra = spectra.reshape(rows, MZ * MOB)
    highest = lax.Precision.HIGHEST
    basis, profiles = (basis_init, profile_init)
    for step in range(ITERS):
        partial_h = lax.dot_general(
            basis.astype(jnp.bfloat16),
            spectra,
            (((0,), (0,)), ((), ())),
            preferred_element_type=jnp.float32,
        )
        partial_gram = lax.dot_general(
            basis,
            basis,
            (((0,), (0,)), ((), ())),
            precision=highest,
            preferred_element_type=jnp.float32,
        )
        shared, gram_feat = scatter_once(partial_h, partial_gram, "feat", n_feat)
        both = halve_sum(jnp.concatenate([shared, gram_feat], axis=1), n_pix, n_feat)
        width = shared.shape[1]
        numer_h = both[:, :width]
        gram_w = both[:, width:]
        profiles = (
            profiles
            * numer_h
            / (
                jnp.dot(gram_w, profiles, precision=highest, preferred_element_type=jnp.float32)
                + EPS
            )
        )
        local_gram = lax.dot_general(
            profiles,
            profiles,
            (((1,), (1,)), ((), ())),
            precision=highest,
            preferred_element_type=jnp.float32,
        )
        profiles_all, gram_h = double_gather(profiles.astype(jnp.bfloat16), local_gram, "feat", n_feat)
        numer_w = lax.dot_general(
            spectra,
            profiles_all,
            (((1,), (1,)), ((), ())),
            preferred_element_type=jnp.float32,
        )
        basis = (
            basis
            * numer_w
            / (jnp.dot(basis, gram_h, precision=highest, preferred_element_type=jnp.float32) + EPS)
        )
    return (basis, profiles)


def solution(mesh):
    return jax.shard_map(
        local,
        mesh=mesh,
        in_specs=(
            P(("pix", "feat"), None),
            P(("pix", "feat"), None),
            P(("pix", "feat"), None),
            P(("pix", "feat"), None),
            P(None, "feat"),
        ),
        out_specs=(P(("pix", "feat"), None), P(None, "feat")),
        check_vma=False,
    )
```

```python
import math

import jax
import jax.numpy as jnp
from jax import lax
from jax.sharding import PartitionSpec as P

MZ = 256
MOB = 16
PEAKS = 256
ITERS = 2
SIDE = 64


EPS = 1e-06


def bin_block(args):
    mass, mobility, weight = args
    feature = mobility * MZ + mass
    hi = feature // SIDE
    lo = feature % SIDE
    side = jnp.arange(SIDE, dtype=jnp.int32)
    hi_hot = (hi[:, :, None] == side[None, None, :]).astype(jnp.bfloat16) * weight[:, :, None]
    lo_hot = (lo[:, :, None] == side[None, None, :]).astype(jnp.bfloat16)
    dense = jnp.einsum("pkh,pkl->phl", hi_hot, lo_hot, preferred_element_type=jnp.float32)
    return dense.reshape(mass.shape[0], MZ * MOB).astype(jnp.bfloat16)


def pairs(n, s):
    return [(i, i ^ s) for i in range(n)]


def scatter_once(x, g, axis, n):
    j = lax.axis_index(axis)
    w = x.shape[1] // n
    x = jnp.roll(x, -j * w, axis=1)
    acc = jnp.concatenate([x[:, :w], g], axis=1)
    for t in range(1, n):
        send = jnp.concatenate([x[:, t * w : (t + 1) * w], g], axis=1)
        acc = acc + lax.ppermute(send, axis, [(i, (i + t) % n) for i in range(n)])
    return acc[:, :w], acc[:, w:]


CORE_BITS = ((0, 2, 3, 4, 1), (2, 0, 1, 3, 4))


def core_pairs(n_pix, n_feat, s):
    out = []
    for d in range(n_pix * n_feat):
        p, f = divmod(d, n_feat)
        bit = CORE_BITS[f % 2][s]
        out.append((d, (p ^ (1 << bit)) * n_feat + f))
    return out


def halve_sum(x, n_pix, n_feat):
    axes = ("pix", "feat")
    p = lax.axis_index("pix")
    core = lax.axis_index("feat") % 2
    first = jnp.where(core == 0, 1 << CORE_BITS[0][0], 1 << CORE_BITS[1][0])
    half = x.shape[1] // 2
    bit = (p // first) % 2
    keep = lax.dynamic_slice_in_dim(x, bit * half, half, axis=1)
    send = lax.dynamic_slice_in_dim(x, (1 - bit) * half, half, axis=1)
    x = keep + lax.ppermute(send, axes, core_pairs(n_pix, n_feat, 0))
    for s in range(1, len(CORE_BITS[0])):
        x = x + lax.ppermute(x, axes, core_pairs(n_pix, n_feat, s))
    other = lax.ppermute(x, axes, core_pairs(n_pix, n_feat, 0))
    return jnp.where(bit == 1, jnp.concatenate([other, x], axis=1), jnp.concatenate([x, other], axis=1))


def exchange_sum(x, g, n_pix, n_feat):
    rows = x.shape[0]
    r = rows // n_pix
    w = x.shape[1] // n_feat
    xs = x.reshape(n_pix, r, n_feat, w).transpose(0, 2, 1, 3)
    gs = jnp.broadcast_to(g.reshape(n_pix, 1, r, g.shape[1]), (n_pix, n_feat, r, g.shape[1]))
    parts = jnp.concatenate([xs, gs], axis=3).reshape(n_pix * n_feat, r, w + g.shape[1])
    got = lax.all_to_all(parts, ("pix", "feat"), 0, 0, tiled=True)
    total = jnp.sum(got, axis=0)
    back = lax.all_to_all(jnp.broadcast_to(total[None], (n_pix,) + total.shape), "pix", 0, 0, tiled=True)
    return back.reshape(rows, w + g.shape[1])


def double_gather(x, g, axis, n):
    j = lax.axis_index(axis)
    s = 1
    while s < n:
        other, got_g = lax.ppermute((x, g), axis, pairs(n, s))
        bit = (j // s) % 2
        x = jnp.where(bit == 1, jnp.concatenate([other, x], axis=1), jnp.concatenate([x, other], axis=1))
        g = g + got_g
        s *= 2
    return x, g


def local(mass_bin, mobility_bin, intensity, basis_init, profile_init):
    n_pix = lax.psum(1, "pix")
    n_feat = lax.psum(1, "feat")
    rows = mass_bin.shape[0]
    block = math.gcd(rows, 1024)
    count = rows // block
    spectra = lax.map(
        bin_block,
        (
            mass_bin.reshape(count, block, PEAKS),
            mobility_bin.reshape(count, block, PEAKS),
            intensity.reshape(count, block, PEAKS),
        ),
    )
    spectra = spectra.reshape(rows, MZ * MOB)
    highest = lax.Precision.HIGHEST
    basis, profiles = (basis_init, profile_init)
    for step in range(ITERS):
        partial_h = lax.dot_general(
            basis.astype(jnp.bfloat16),
            spectra,
            (((0,), (0,)), ((), ())),
            preferred_element_type=jnp.float32,
        )
        partial_gram = lax.dot_general(
            basis,
            basis,
            (((0,), (0,)), ((), ())),
            precision=highest,
            preferred_element_type=jnp.float32,
        )
        both = exchange_sum(partial_h, partial_gram, n_pix, n_feat)
        width = partial_h.shape[1] // n_feat
        numer_h = both[:, :width]
        gram_w = both[:, width:]
        profiles = (
            profiles
            * numer_h
            / (
                jnp.dot(gram_w, profiles, precision=highest, preferred_element_type=jnp.float32)
                + EPS
            )
        )
        local_gram = lax.dot_general(
            profiles,
            profiles,
            (((1,), (1,)), ((), ())),
            precision=highest,
            preferred_element_type=jnp.float32,
        )
        profiles_all, gram_h = double_gather(profiles.astype(jnp.bfloat16), local_gram, "feat", n_feat)
        numer_w = lax.dot_general(
            spectra,
            profiles_all,
            (((1,), (1,)), ((), ())),
            preferred_element_type=jnp.float32,
        )
        basis = (
            basis
            * numer_w
            / (jnp.dot(basis, gram_h, precision=highest, preferred_element_type=jnp.float32) + EPS)
        )
    return (basis, profiles)


def solution(mesh):
    return jax.shard_map(
        local,
        mesh=mesh,
        in_specs=(
            P(("pix", "feat"), None),
            P(("pix", "feat"), None),
            P(("pix", "feat"), None),
            P(("pix", "feat"), None),
            P(None, "feat"),
        ),
        out_specs=(P(("pix", "feat"), None), P(None, "feat")),
        check_vma=False,
    )
```

```python
import math

import jax
import jax.numpy as jnp
from jax import lax
from jax.sharding import PartitionSpec as P

MZ = 256
MOB = 16
PEAKS = 256
ITERS = 2
SIDE = 64


EPS = 1e-06


def bin_block(args):
    mass, mobility, weight = args
    feature = mobility * MZ + mass
    hi = feature // SIDE
    lo = feature % SIDE
    side = jnp.arange(SIDE, dtype=jnp.int32)
    hi_hot = (hi[:, :, None] == side[None, None, :]).astype(jnp.bfloat16) * weight[:, :, None]
    lo_hot = (lo[:, :, None] == side[None, None, :]).astype(jnp.bfloat16)
    dense = jnp.einsum("pkh,pkl->phl", hi_hot, lo_hot, preferred_element_type=jnp.float32)
    return dense.reshape(mass.shape[0], MZ * MOB).astype(jnp.bfloat16)


def pairs(n, s):
    return [(i, i ^ s) for i in range(n)]


def scatter_once(x, g, axis, n):
    j = lax.axis_index(axis)
    w = x.shape[1] // n
    x = jnp.roll(x, -j * w, axis=1)
    acc = jnp.concatenate([x[:, :w], g], axis=1)
    for t in range(1, n):
        send = jnp.concatenate([x[:, t * w : (t + 1) * w], g], axis=1)
        acc = acc + lax.ppermute(send, axis, [(i, (i + t) % n) for i in range(n)])
    return acc[:, :w], acc[:, w:]


CORE_BITS = ((0, 2, 3, 4, 1), (2, 0, 1, 3, 4))


def core_pairs(n_pix, n_feat, s):
    out = []
    for d in range(n_pix * n_feat):
        p, f = divmod(d, n_feat)
        bit = CORE_BITS[f % 2][s]
        out.append((d, (p ^ (1 << bit)) * n_feat + f))
    return out


def halve_sum(x, n_pix, n_feat):
    axes = ("pix", "feat")
    p = lax.axis_index("pix")
    core = lax.axis_index("feat") % 2
    first = jnp.where(core == 0, 1 << CORE_BITS[0][0], 1 << CORE_BITS[1][0])
    half = x.shape[1] // 2
    bit = (p // first) % 2
    keep = lax.dynamic_slice_in_dim(x, bit * half, half, axis=1)
    send = lax.dynamic_slice_in_dim(x, (1 - bit) * half, half, axis=1)
    x = keep + lax.ppermute(send, axes, core_pairs(n_pix, n_feat, 0))
    for s in range(1, len(CORE_BITS[0])):
        x = x + lax.ppermute(x, axes, core_pairs(n_pix, n_feat, s))
    other = lax.ppermute(x, axes, core_pairs(n_pix, n_feat, 0))
    return jnp.where(bit == 1, jnp.concatenate([other, x], axis=1), jnp.concatenate([x, other], axis=1))


def exchange_sum(x, axis, n):
    rows = x.shape[0]
    got = lax.all_to_all(x.reshape(n, rows // n, x.shape[1]), axis, 0, 0, tiled=True)
    total = jnp.sum(got, axis=0)
    back = lax.all_to_all(jnp.broadcast_to(total[None], (n,) + total.shape), axis, 0, 0, tiled=True)
    return back.reshape(rows, x.shape[1])


def double_gather(x, g, axis, n):
    j = lax.axis_index(axis)
    s = 1
    while s < n:
        other, got_g = lax.ppermute((x, g), axis, pairs(n, s))
        bit = (j // s) % 2
        x = jnp.where(bit == 1, jnp.concatenate([other, x], axis=1), jnp.concatenate([x, other], axis=1))
        g = g + got_g
        s *= 2
    return x, g


def local(mass_bin, mobility_bin, intensity, basis_init, profile_init):
    n_pix = lax.psum(1, "pix")
    n_feat = lax.psum(1, "feat")
    rows = mass_bin.shape[0]
    block = math.gcd(rows, 1024)
    count = rows // block
    spectra = lax.map(
        bin_block,
        (
            mass_bin.reshape(count, block, PEAKS),
            mobility_bin.reshape(count, block, PEAKS),
            intensity.reshape(count, block, PEAKS),
        ),
    )
    spectra = spectra.reshape(rows, MZ * MOB)
    highest = lax.Precision.HIGHEST
    basis, profiles = (basis_init, profile_init)
    for step in range(ITERS):
        partial_h = lax.dot_general(
            basis.astype(jnp.bfloat16),
            spectra,
            (((0,), (0,)), ((), ())),
            preferred_element_type=jnp.float32,
        )
        partial_gram = lax.dot_general(
            basis,
            basis,
            (((0,), (0,)), ((), ())),
            precision=highest,
            preferred_element_type=jnp.float32,
        )
        shared, gram_feat = scatter_once(partial_h, partial_gram, "feat", n_feat)
        both = exchange_sum(jnp.concatenate([shared, gram_feat], axis=1), "pix", n_pix)
        width = shared.shape[1]
        numer_h = both[:, :width]
        gram_w = both[:, width:]
        profiles = (
            profiles
            * numer_h
            / (
                jnp.dot(gram_w, profiles, precision=highest, preferred_element_type=jnp.float32)
                + EPS
            )
        )
        local_gram = lax.dot_general(
            profiles,
            profiles,
            (((1,), (1,)), ((), ())),
            precision=highest,
            preferred_element_type=jnp.float32,
        )
        profiles_all, gram_h = double_gather(profiles.astype(jnp.bfloat16), local_gram, "feat", n_feat)
        numer_w = lax.dot_general(
            spectra,
            profiles_all,
            (((1,), (1,)), ((), ())),
            preferred_element_type=jnp.float32,
        )
        basis = (
            basis
            * numer_w
            / (jnp.dot(basis, gram_h, precision=highest, preferred_element_type=jnp.float32) + EPS)
        )
    return (basis, profiles)


def solution(mesh):
    return jax.shard_map(
        local,
        mesh=mesh,
        in_specs=(
            P(("pix", "feat"), None),
            P(("pix", "feat"), None),
            P(("pix", "feat"), None),
            P(("pix", "feat"), None),
            P(None, "feat"),
        ),
        out_specs=(P(("pix", "feat"), None), P(None, "feat")),
        check_vma=False,
    )
```

```python
import math

import jax
import jax.numpy as jnp
from jax import lax
from jax.sharding import PartitionSpec as P

MZ = 256
MOB = 16
PEAKS = 256
ITERS = 2
SIDE = 64


EPS = 1e-06


def bin_block(args):
    mass, mobility, weight = args
    feature = mobility * MZ + mass
    hi = feature // SIDE
    lo = feature % SIDE
    side = jnp.arange(SIDE, dtype=jnp.int32)
    hi_hot = (hi[:, :, None] == side[None, None, :]).astype(jnp.bfloat16) * weight[:, :, None]
    lo_hot = (lo[:, :, None] == side[None, None, :]).astype(jnp.bfloat16)
    dense = jnp.einsum("pkh,pkl->phl", hi_hot, lo_hot, preferred_element_type=jnp.float32)
    return dense.reshape(mass.shape[0], MZ * MOB).astype(jnp.bfloat16)


def pairs(n, s):
    return [(i, i ^ s) for i in range(n)]


def scatter_once(x, g, axis, n):
    j = lax.axis_index(axis)
    w = x.shape[1] // n
    x = jnp.roll(x, -j * w, axis=1)
    acc = jnp.concatenate([x[:, :w], g], axis=1)
    for t in range(1, n):
        send = jnp.concatenate([x[:, t * w : (t + 1) * w], g], axis=1)
        acc = acc + lax.ppermute(send, axis, [(i, (i + t) % n) for i in range(n)])
    return acc[:, :w], acc[:, w:]


CORE_BITS = ((0, 2, 3, 4, 1), (2, 0, 1, 3, 4))


def core_pairs(n_pix, n_feat, s):
    out = []
    for d in range(n_pix * n_feat):
        p, f = divmod(d, n_feat)
        bit = CORE_BITS[f % 2][s]
        out.append((d, (p ^ (1 << bit)) * n_feat + f))
    return out


def halve_sum(x, n_pix, n_feat):
    axes = ("pix", "feat")
    p = lax.axis_index("pix")
    core = lax.axis_index("feat") % 2
    first = jnp.where(core == 0, 1 << CORE_BITS[0][0], 1 << CORE_BITS[1][0])
    half = x.shape[1] // 2
    bit = (p // first) % 2
    keep = lax.dynamic_slice_in_dim(x, bit * half, half, axis=1)
    send = lax.dynamic_slice_in_dim(x, (1 - bit) * half, half, axis=1)
    x = keep + lax.ppermute(send, axes, core_pairs(n_pix, n_feat, 0))
    for s in range(1, len(CORE_BITS[0])):
        x = x + lax.ppermute(x, axes, core_pairs(n_pix, n_feat, s))
    other = lax.ppermute(x, axes, core_pairs(n_pix, n_feat, 0))
    return jnp.where(bit == 1, jnp.concatenate([other, x], axis=1), jnp.concatenate([x, other], axis=1))


def exchange_sum(x, axis, n):
    rows = x.shape[0]
    got = lax.all_to_all(x.reshape(n, rows // n, x.shape[1]), axis, 0, 0, tiled=True)
    total = jnp.sum(got, axis=0)
    back = lax.all_to_all(jnp.broadcast_to(total[None], (n,) + total.shape), axis, 0, 0, tiled=True)
    return back.reshape(rows, x.shape[1])


def exchange_scatter(x, g, axis, n):
    w = x.shape[1] // n
    blocks = x.reshape(x.shape[0], n, w).transpose(1, 0, 2)
    blocks = jnp.concatenate([blocks, jnp.broadcast_to(g[None], (n,) + g.shape)], axis=2)
    total = jnp.sum(lax.all_to_all(blocks, axis, 0, 0, tiled=True), axis=0)
    return total[:, :w], total[:, w:]


def double_gather(x, g, axis, n):
    j = lax.axis_index(axis)
    s = 1
    while s < n:
        other, got_g = lax.ppermute((x, g), axis, pairs(n, s))
        bit = (j // s) % 2
        x = jnp.where(bit == 1, jnp.concatenate([other, x], axis=1), jnp.concatenate([x, other], axis=1))
        g = g + got_g
        s *= 2
    return x, g


def local(mass_bin, mobility_bin, intensity, basis_init, profile_init):
    n_pix = lax.psum(1, "pix")
    n_feat = lax.psum(1, "feat")
    rows = mass_bin.shape[0]
    block = math.gcd(rows, 1024)
    count = rows // block
    spectra = lax.map(
        bin_block,
        (
            mass_bin.reshape(count, block, PEAKS),
            mobility_bin.reshape(count, block, PEAKS),
            intensity.reshape(count, block, PEAKS),
        ),
    )
    spectra = spectra.reshape(rows, MZ * MOB)
    highest = lax.Precision.HIGHEST
    basis, profiles = (basis_init, profile_init)
    for step in range(ITERS):
        partial_h = lax.dot_general(
            basis.astype(jnp.bfloat16),
            spectra,
            (((0,), (0,)), ((), ())),
            preferred_element_type=jnp.float32,
        )
        partial_gram = lax.dot_general(
            basis,
            basis,
            (((0,), (0,)), ((), ())),
            precision=highest,
            preferred_element_type=jnp.float32,
        )
        shared, gram_feat = exchange_scatter(partial_h, partial_gram, "feat", n_feat)
        both = exchange_sum(jnp.concatenate([shared, gram_feat], axis=1), "pix", n_pix)
        width = shared.shape[1]
        numer_h = both[:, :width]
        gram_w = both[:, width:]
        profiles = (
            profiles
            * numer_h
            / (
                jnp.dot(gram_w, profiles, precision=highest, preferred_element_type=jnp.float32)
                + EPS
            )
        )
        local_gram = lax.dot_general(
            profiles,
            profiles,
            (((1,), (1,)), ((), ())),
            precision=highest,
            preferred_element_type=jnp.float32,
        )
        profiles_all, gram_h = double_gather(profiles.astype(jnp.bfloat16), local_gram, "feat", n_feat)
        numer_w = lax.dot_general(
            spectra,
            profiles_all,
            (((1,), (1,)), ((), ())),
            preferred_element_type=jnp.float32,
        )
        basis = (
            basis
            * numer_w
            / (jnp.dot(basis, gram_h, precision=highest, preferred_element_type=jnp.float32) + EPS)
        )
    return (basis, profiles)


def solution(mesh):
    return jax.shard_map(
        local,
        mesh=mesh,
        in_specs=(
            P(("pix", "feat"), None),
            P(("pix", "feat"), None),
            P(("pix", "feat"), None),
            P(("pix", "feat"), None),
            P(None, "feat"),
        ),
        out_specs=(P(("pix", "feat"), None), P(None, "feat")),
        check_vma=False,
    )
```

```python
import math

import jax
import jax.numpy as jnp
from jax import lax
from jax.sharding import PartitionSpec as P

MZ = 256
MOB = 16
PEAKS = 256
ITERS = 2
SIDE = 64


EPS = 1e-06


def bin_block(args):
    mass, mobility, weight = args
    feature = mobility * MZ + mass
    hi = feature // SIDE
    lo = feature % SIDE
    side = jnp.arange(SIDE, dtype=jnp.int32)
    hi_hot = (hi[:, :, None] == side[None, None, :]).astype(jnp.bfloat16) * weight[:, :, None]
    lo_hot = (lo[:, :, None] == side[None, None, :]).astype(jnp.bfloat16)
    dense = jnp.einsum("pkh,pkl->phl", hi_hot, lo_hot, preferred_element_type=jnp.float32)
    return dense.reshape(mass.shape[0], MZ * MOB).astype(jnp.bfloat16)


def pairs(n, s):
    return [(i, i ^ s) for i in range(n)]


def scatter_once(x, g, axis, n):
    j = lax.axis_index(axis)
    w = x.shape[1] // n
    x = jnp.roll(x, -j * w, axis=1)
    acc = jnp.concatenate([x[:, :w], g], axis=1)
    for t in range(1, n):
        send = jnp.concatenate([x[:, t * w : (t + 1) * w], g], axis=1)
        acc = acc + lax.ppermute(send, axis, [(i, (i + t) % n) for i in range(n)])
    return acc[:, :w], acc[:, w:]


CORE_BITS = ((0, 2, 3, 4, 1), (2, 0, 1, 3, 4))


def core_pairs(n_pix, n_feat, s):
    out = []
    for d in range(n_pix * n_feat):
        p, f = divmod(d, n_feat)
        bit = CORE_BITS[f % 2][s]
        out.append((d, (p ^ (1 << bit)) * n_feat + f))
    return out


def halve_sum(x, n_pix, n_feat):
    axes = ("pix", "feat")
    p = lax.axis_index("pix")
    core = lax.axis_index("feat") % 2
    first = jnp.where(core == 0, 1 << CORE_BITS[0][0], 1 << CORE_BITS[1][0])
    half = x.shape[1] // 2
    bit = (p // first) % 2
    keep = lax.dynamic_slice_in_dim(x, bit * half, half, axis=1)
    send = lax.dynamic_slice_in_dim(x, (1 - bit) * half, half, axis=1)
    x = keep + lax.ppermute(send, axes, core_pairs(n_pix, n_feat, 0))
    for s in range(1, len(CORE_BITS[0])):
        x = x + lax.ppermute(x, axes, core_pairs(n_pix, n_feat, s))
    other = lax.ppermute(x, axes, core_pairs(n_pix, n_feat, 0))
    return jnp.where(bit == 1, jnp.concatenate([other, x], axis=1), jnp.concatenate([x, other], axis=1))


def exchange_sum(x, axis, n):
    rows = x.shape[0]
    got = lax.all_to_all(x.reshape(n, rows // n, x.shape[1]), axis, 0, 0, tiled=True)
    total = jnp.sum(got, axis=0)
    back = lax.all_to_all(jnp.broadcast_to(total[None], (n,) + total.shape), axis, 0, 0, tiled=True)
    return back.reshape(rows, x.shape[1])


def exchange_gather(x, axis, n):
    xs = lax.all_to_all(jnp.broadcast_to(x[None], (n,) + x.shape), axis, 0, 0, tiled=True)
    return xs.transpose(1, 0, 2).reshape(x.shape[0], n * x.shape[1])


def double_sum(x, axis, n):
    s = 1
    while s < n:
        x = x + lax.ppermute(x, axis, pairs(n, s))
        s *= 2
    return x


def double_gather(x, g, axis, n):
    j = lax.axis_index(axis)
    s = 1
    while s < n:
        other, got_g = lax.ppermute((x, g), axis, pairs(n, s))
        bit = (j // s) % 2
        x = jnp.where(bit == 1, jnp.concatenate([other, x], axis=1), jnp.concatenate([x, other], axis=1))
        g = g + got_g
        s *= 2
    return x, g


def local(mass_bin, mobility_bin, intensity, basis_init, profile_init):
    n_pix = lax.psum(1, "pix")
    n_feat = lax.psum(1, "feat")
    rows = mass_bin.shape[0]
    block = math.gcd(rows, 1024)
    count = rows // block
    spectra = lax.map(
        bin_block,
        (
            mass_bin.reshape(count, block, PEAKS),
            mobility_bin.reshape(count, block, PEAKS),
            intensity.reshape(count, block, PEAKS),
        ),
    )
    spectra = spectra.reshape(rows, MZ * MOB)
    highest = lax.Precision.HIGHEST
    basis, profiles = (basis_init, profile_init)
    for step in range(ITERS):
        partial_h = lax.dot_general(
            basis.astype(jnp.bfloat16),
            spectra,
            (((0,), (0,)), ((), ())),
            preferred_element_type=jnp.float32,
        )
        partial_gram = lax.dot_general(
            basis,
            basis,
            (((0,), (0,)), ((), ())),
            precision=highest,
            preferred_element_type=jnp.float32,
        )
        shared, gram_feat = scatter_once(partial_h, partial_gram, "feat", n_feat)
        both = exchange_sum(jnp.concatenate([shared, gram_feat], axis=1), "pix", n_pix)
        width = shared.shape[1]
        numer_h = both[:, :width]
        gram_w = both[:, width:]
        profiles = (
            profiles
            * numer_h
            / (
                jnp.dot(gram_w, profiles, precision=highest, preferred_element_type=jnp.float32)
                + EPS
            )
        )
        local_gram = lax.dot_general(
            profiles,
            profiles,
            (((1,), (1,)), ((), ())),
            precision=highest,
            preferred_element_type=jnp.float32,
        )
        profiles_all = exchange_gather(profiles.astype(jnp.bfloat16), "feat", n_feat)
        gram_h = double_sum(local_gram, "feat", n_feat)
        numer_w = lax.dot_general(
            spectra,
            profiles_all,
            (((1,), (1,)), ((), ())),
            preferred_element_type=jnp.float32,
        )
        basis = (
            basis
            * numer_w
            / (jnp.dot(basis, gram_h, precision=highest, preferred_element_type=jnp.float32) + EPS)
        )
    return (basis, profiles)


def solution(mesh):
    return jax.shard_map(
        local,
        mesh=mesh,
        in_specs=(
            P(("pix", "feat"), None),
            P(("pix", "feat"), None),
            P(("pix", "feat"), None),
            P(("pix", "feat"), None),
            P(None, "feat"),
        ),
        out_specs=(P(("pix", "feat"), None), P(None, "feat")),
        check_vma=False,
    )
```

```python
import math

import jax
import jax.numpy as jnp
from jax import lax
from jax.sharding import PartitionSpec as P

MZ = 256
MOB = 16
PEAKS = 256
ITERS = 2
SIDE = 64


EPS = 1e-06


def bin_block(args):
    mass, mobility, weight = args
    feature = mobility * MZ + mass
    hi = feature // SIDE
    lo = feature % SIDE
    side = jnp.arange(SIDE, dtype=jnp.int32)
    hi_hot = (hi[:, :, None] == side[None, None, :]).astype(jnp.bfloat16) * weight[:, :, None]
    lo_hot = (lo[:, :, None] == side[None, None, :]).astype(jnp.bfloat16)
    dense = jnp.einsum("pkh,pkl->phl", hi_hot, lo_hot, preferred_element_type=jnp.float32)
    return dense.reshape(mass.shape[0], MZ * MOB).astype(jnp.bfloat16)


def pairs(n, s):
    return [(i, i ^ s) for i in range(n)]


def scatter_once(x, g, axis, n):
    j = lax.axis_index(axis)
    w = x.shape[1] // n
    x = jnp.roll(x, -j * w, axis=1)
    acc = jnp.concatenate([x[:, :w], g], axis=1)
    for t in range(1, n):
        send = jnp.concatenate([x[:, t * w : (t + 1) * w], g], axis=1)
        acc = acc + lax.ppermute(send, axis, [(i, (i + t) % n) for i in range(n)])
    return acc[:, :w], acc[:, w:]


CORE_BITS = ((0, 2, 3, 4, 1), (2, 0, 1, 3, 4))


def core_pairs(n_pix, n_feat, s):
    out = []
    for d in range(n_pix * n_feat):
        p, f = divmod(d, n_feat)
        bit = CORE_BITS[f % 2][s]
        out.append((d, (p ^ (1 << bit)) * n_feat + f))
    return out


def halve_sum(x, n_pix, n_feat):
    axes = ("pix", "feat")
    p = lax.axis_index("pix")
    core = lax.axis_index("feat") % 2
    first = jnp.where(core == 0, 1 << CORE_BITS[0][0], 1 << CORE_BITS[1][0])
    half = x.shape[1] // 2
    bit = (p // first) % 2
    keep = lax.dynamic_slice_in_dim(x, bit * half, half, axis=1)
    send = lax.dynamic_slice_in_dim(x, (1 - bit) * half, half, axis=1)
    x = keep + lax.ppermute(send, axes, core_pairs(n_pix, n_feat, 0))
    for s in range(1, len(CORE_BITS[0])):
        x = x + lax.ppermute(x, axes, core_pairs(n_pix, n_feat, s))
    other = lax.ppermute(x, axes, core_pairs(n_pix, n_feat, 0))
    return jnp.where(bit == 1, jnp.concatenate([other, x], axis=1), jnp.concatenate([x, other], axis=1))


def rows_sum(x, axis, n):
    rows = x.shape[0]
    got = lax.all_to_all(x.reshape(n, rows // n, x.shape[1]), axis, 0, 0, tiled=True)
    return jnp.sum(got, axis=0)


def rows_gather(x, axis, n):
    back = lax.all_to_all(jnp.broadcast_to(x[None], (n,) + x.shape), axis, 0, 0, tiled=True)
    return back.reshape(n * x.shape[0], x.shape[1])


def double_gather(x, g, axis, n):
    j = lax.axis_index(axis)
    s = 1
    while s < n:
        other, got_g = lax.ppermute((x, g), axis, pairs(n, s))
        bit = (j // s) % 2
        x = jnp.where(bit == 1, jnp.concatenate([other, x], axis=1), jnp.concatenate([x, other], axis=1))
        g = g + got_g
        s *= 2
    return x, g


def local(mass_bin, mobility_bin, intensity, basis_init, profile_init):
    n_pix = lax.psum(1, "pix")
    n_feat = lax.psum(1, "feat")
    rows = mass_bin.shape[0]
    block = math.gcd(rows, 1024)
    count = rows // block
    spectra = lax.map(
        bin_block,
        (
            mass_bin.reshape(count, block, PEAKS),
            mobility_bin.reshape(count, block, PEAKS),
            intensity.reshape(count, block, PEAKS),
        ),
    )
    spectra = spectra.reshape(rows, MZ * MOB)
    highest = lax.Precision.HIGHEST
    basis, profiles = (basis_init, profile_init)
    for step in range(ITERS):
        partial_h = lax.dot_general(
            basis.astype(jnp.bfloat16),
            spectra,
            (((0,), (0,)), ((), ())),
            preferred_element_type=jnp.float32,
        )
        partial_gram = lax.dot_general(
            basis,
            basis,
            (((0,), (0,)), ((), ())),
            precision=highest,
            preferred_element_type=jnp.float32,
        )
        shared, gram_feat = scatter_once(partial_h, partial_gram, "feat", n_feat)
        both = rows_sum(jnp.concatenate([shared, gram_feat], axis=1), "pix", n_pix)
        width = shared.shape[1]
        numer_h = both[:, :width]
        gram_w = both[:, width:]
        mine = lax.dynamic_slice_in_dim(profiles, lax.axis_index("pix") * both.shape[0], both.shape[0], axis=0)
        mine = (
            mine
            * numer_h
            / (
                jnp.dot(gram_w, profiles, precision=highest, preferred_element_type=jnp.float32)
                + EPS
            )
        )
        profiles = rows_gather(mine, "pix", n_pix)
        local_gram = lax.dot_general(
            profiles,
            profiles,
            (((1,), (1,)), ((), ())),
            precision=highest,
            preferred_element_type=jnp.float32,
        )
        profiles_all, gram_h = double_gather(profiles.astype(jnp.bfloat16), local_gram, "feat", n_feat)
        numer_w = lax.dot_general(
            spectra,
            profiles_all,
            (((1,), (1,)), ((), ())),
            preferred_element_type=jnp.float32,
        )
        basis = (
            basis
            * numer_w
            / (jnp.dot(basis, gram_h, precision=highest, preferred_element_type=jnp.float32) + EPS)
        )
    return (basis, profiles)


def solution(mesh):
    return jax.shard_map(
        local,
        mesh=mesh,
        in_specs=(
            P(("pix", "feat"), None),
            P(("pix", "feat"), None),
            P(("pix", "feat"), None),
            P(("pix", "feat"), None),
            P(None, "feat"),
        ),
        out_specs=(P(("pix", "feat"), None), P(None, "feat")),
        check_vma=False,
    )
```

```python
import math

import jax
import jax.numpy as jnp
from jax import lax
from jax.sharding import PartitionSpec as P

MZ = 256
MOB = 16
PEAKS = 256
ITERS = 2
SIDE = 64


EPS = 1e-06


def bin_block(args):
    mass, mobility, weight = args
    feature = mobility * MZ + mass
    hi = feature >> 6
    lo = feature & (SIDE - 1)
    side = jnp.arange(SIDE, dtype=jnp.int32)
    hi_hot = (hi[:, :, None] == side[None, None, :]).astype(jnp.bfloat16) * weight[:, :, None]
    lo_hot = (lo[:, :, None] == side[None, None, :]).astype(jnp.bfloat16)
    dense = jnp.einsum("pkh,pkl->phl", hi_hot, lo_hot, preferred_element_type=jnp.float32)
    return dense.reshape(mass.shape[0], MZ * MOB).astype(jnp.bfloat16)


def pairs(n, s):
    return [(i, i ^ s) for i in range(n)]


def scatter_once(x, g, axis, n):
    j = lax.axis_index(axis)
    core = j % 2
    y = j // 2
    w = x.shape[1] // n
    rows = x.shape[0]
    x = x.reshape(rows, n // 2, 2, w)
    keep = lax.dynamic_index_in_dim(x, core, axis=2, keepdims=False)
    send = lax.dynamic_index_in_dim(x, 1 - core, axis=2, keepdims=False).reshape(rows, (n // 2) * w)
    got = lax.ppermute(jnp.concatenate([send, g], axis=1), axis, pairs(n, 1))
    half = keep + got[:, : (n // 2) * w].reshape(rows, n // 2, w)
    g = g + got[:, (n // 2) * w :]
    half = jnp.roll(half, -y, axis=1)
    acc = jnp.concatenate([half[:, 0], g], axis=1)
    for t in range(1, n // 2):
        msg = jnp.concatenate([half[:, t], g], axis=1)
        acc = acc + lax.ppermute(msg, axis, [(i, (i + 2 * t) % n) for i in range(n)])
    return acc[:, :w], acc[:, w:]


CORE_BITS = ((0, 2, 3, 4, 1), (2, 0, 1, 3, 4))


def core_pairs(n_pix, n_feat, s):
    out = []
    for d in range(n_pix * n_feat):
        p, f = divmod(d, n_feat)
        bit = CORE_BITS[f % 2][s]
        out.append((d, (p ^ (1 << bit)) * n_feat + f))
    return out


def halve_sum(x, n_pix, n_feat):
    axes = ("pix", "feat")
    p = lax.axis_index("pix")
    core = lax.axis_index("feat") % 2
    first = jnp.where(core == 0, 1 << CORE_BITS[0][0], 1 << CORE_BITS[1][0])
    half = x.shape[1] // 2
    bit = (p // first) % 2
    keep = lax.dynamic_slice_in_dim(x, bit * half, half, axis=1)
    send = lax.dynamic_slice_in_dim(x, (1 - bit) * half, half, axis=1)
    x = keep + lax.ppermute(send, axes, core_pairs(n_pix, n_feat, 0))
    for s in range(1, len(CORE_BITS[0])):
        x = x + lax.ppermute(x, axes, core_pairs(n_pix, n_feat, s))
    other = lax.ppermute(x, axes, core_pairs(n_pix, n_feat, 0))
    return jnp.where(bit == 1, jnp.concatenate([other, x], axis=1), jnp.concatenate([x, other], axis=1))


def exchange_sum(x, axis, n):
    rows = x.shape[0]
    got = lax.all_to_all(x.reshape(n, rows // n, x.shape[1]), axis, 0, 0, tiled=True)
    total = jnp.sum(got, axis=0)
    back = lax.all_to_all(jnp.broadcast_to(total[None], (n,) + total.shape), axis, 0, 0, tiled=True)
    return back.reshape(rows, x.shape[1])


def double_gather(x, g, axis, n):
    j = lax.axis_index(axis)
    s = 1
    while s < n:
        other, got_g = lax.ppermute((x, g), axis, pairs(n, s))
        bit = (j // s) % 2
        x = jnp.where(bit == 1, jnp.concatenate([other, x], axis=1), jnp.concatenate([x, other], axis=1))
        g = g + got_g
        s *= 2
    return x, g


def local(mass_bin, mobility_bin, intensity, basis_init, profile_init):
    n_pix = lax.psum(1, "pix")
    n_feat = lax.psum(1, "feat")
    rows = mass_bin.shape[0]
    block = math.gcd(rows, 1024)
    count = rows // block
    spectra = lax.map(
        bin_block,
        (
            mass_bin.reshape(count, block, PEAKS),
            mobility_bin.reshape(count, block, PEAKS),
            intensity.reshape(count, block, PEAKS),
        ),
    )
    spectra = spectra.reshape(rows, MZ * MOB)
    highest = lax.Precision.HIGHEST
    basis, profiles = (basis_init, profile_init)
    for step in range(ITERS):
        partial_h = lax.dot_general(
            basis.astype(jnp.bfloat16),
            spectra,
            (((0,), (0,)), ((), ())),
            preferred_element_type=jnp.float32,
        )
        partial_gram = lax.dot_general(
            basis,
            basis,
            (((0,), (0,)), ((), ())),
            precision=highest,
            preferred_element_type=jnp.float32,
        )
        shared, gram_feat = scatter_once(partial_h, partial_gram, "feat", n_feat)
        both = exchange_sum(jnp.concatenate([shared, gram_feat], axis=1), "pix", n_pix)
        width = shared.shape[1]
        numer_h = both[:, :width]
        gram_w = both[:, width:]
        profiles = (
            profiles
            * numer_h
            / (
                jnp.dot(gram_w, profiles, precision=highest, preferred_element_type=jnp.float32)
                + EPS
            )
        )
        local_gram = lax.dot_general(
            profiles,
            profiles,
            (((1,), (1,)), ((), ())),
            precision=highest,
            preferred_element_type=jnp.float32,
        )
        profiles_all, gram_h = double_gather(profiles.astype(jnp.bfloat16), local_gram, "feat", n_feat)
        numer_w = lax.dot_general(
            spectra,
            profiles_all,
            (((1,), (1,)), ((), ())),
            preferred_element_type=jnp.float32,
        )
        basis = (
            basis
            * numer_w
            / (jnp.dot(basis, gram_h, precision=highest, preferred_element_type=jnp.float32) + EPS)
        )
    return (basis, profiles)


def solution(mesh):
    return jax.shard_map(
        local,
        mesh=mesh,
        in_specs=(
            P(("pix", "feat"), None),
            P(("pix", "feat"), None),
            P(("pix", "feat"), None),
            P(("pix", "feat"), None),
            P(None, "feat"),
        ),
        out_specs=(P(("pix", "feat"), None), P(None, "feat")),
        check_vma=False,
    )
```

```python
import math

import jax
import jax.numpy as jnp
from jax import lax
from jax.sharding import PartitionSpec as P

MZ = 256
MOB = 16
PEAKS = 256
ITERS = 2
SIDE = 64


EPS = 1e-06


def bin_block(args):
    mass, mobility, weight = args
    feature = mobility * MZ + mass
    hi = feature >> 6
    lo = feature & (SIDE - 1)
    side = jnp.arange(SIDE, dtype=jnp.int32)
    hi_hot = (hi[:, :, None] == side[None, None, :]).astype(jnp.bfloat16) * weight[:, :, None]
    lo_hot = (lo[:, :, None] == side[None, None, :]).astype(jnp.bfloat16)
    dense = jnp.einsum("pkh,pkl->phl", hi_hot, lo_hot, preferred_element_type=jnp.float32)
    return dense.reshape(mass.shape[0], MZ * MOB).astype(jnp.bfloat16)


def pairs(n, s):
    return [(i, i ^ s) for i in range(n)]


def scatter_once(x, g, axis, n):
    j = lax.axis_index(axis)
    core = j % 2
    y = j // 2
    w = x.shape[1] // n
    rows = x.shape[0]
    x = x.reshape(rows, n // 2, 2, w)
    keep = lax.dynamic_index_in_dim(x, core, axis=2, keepdims=False)
    send = lax.dynamic_index_in_dim(x, 1 - core, axis=2, keepdims=False).reshape(rows, (n // 2) * w)
    got = lax.ppermute(jnp.concatenate([send, g], axis=1), axis, pairs(n, 1))
    half = keep + got[:, : (n // 2) * w].reshape(rows, n // 2, w)
    g = g + got[:, (n // 2) * w :]
    half = jnp.roll(half, -y, axis=1)
    acc = jnp.concatenate([half[:, 0], g], axis=1)
    for t in range(1, n // 2):
        msg = jnp.concatenate([half[:, t], g], axis=1)
        acc = acc + lax.ppermute(msg, axis, [(i, (i + 2 * t) % n) for i in range(n)])
    return acc[:, :w], acc[:, w:]


CORE_BITS = ((0, 2, 3, 4, 1), (2, 0, 1, 3, 4))


def core_pairs(n_pix, n_feat, s):
    out = []
    for d in range(n_pix * n_feat):
        p, f = divmod(d, n_feat)
        bit = CORE_BITS[f % 2][s]
        out.append((d, (p ^ (1 << bit)) * n_feat + f))
    return out


def halve_sum(x, n_pix, n_feat):
    axes = ("pix", "feat")
    p = lax.axis_index("pix")
    core = lax.axis_index("feat") % 2
    first = jnp.where(core == 0, 1 << CORE_BITS[0][0], 1 << CORE_BITS[1][0])
    half = x.shape[1] // 2
    bit = (p // first) % 2
    keep = lax.dynamic_slice_in_dim(x, bit * half, half, axis=1)
    send = lax.dynamic_slice_in_dim(x, (1 - bit) * half, half, axis=1)
    x = keep + lax.ppermute(send, axes, core_pairs(n_pix, n_feat, 0))
    for s in range(1, len(CORE_BITS[0])):
        x = x + lax.ppermute(x, axes, core_pairs(n_pix, n_feat, s))
    other = lax.ppermute(x, axes, core_pairs(n_pix, n_feat, 0))
    return jnp.where(bit == 1, jnp.concatenate([other, x], axis=1), jnp.concatenate([x, other], axis=1))


def exchange_sum(x, axis, n):
    rows = x.shape[0]
    got = lax.all_to_all(x.reshape(n, rows // n, x.shape[1]), axis, 0, 0, tiled=True)
    total = jnp.sum(got, axis=0)
    back = lax.all_to_all(jnp.broadcast_to(total[None], (n,) + total.shape), axis, 0, 0, tiled=True)
    return back.reshape(rows, x.shape[1])


def double_gather(x, g, axis, n):
    j = lax.axis_index(axis)
    core = j % 2
    y = j // 2
    other, got_g = lax.ppermute((x, g), axis, pairs(n, 1))
    x = jnp.where(core == 1, jnp.concatenate([other, x], axis=1), jnp.concatenate([x, other], axis=1))
    g = g + got_g
    parts = [x]
    total = g
    for t in range(1, n // 2):
        a, b = lax.ppermute((x, g), axis, [(i, (i + 2 * t) % n) for i in range(n)])
        parts.append(a)
        total = total + b
    stack = jnp.stack(parts)
    canon = jnp.take(stack, (y - jnp.arange(n // 2)) % (n // 2), axis=0)
    return jnp.concatenate([canon[c] for c in range(n // 2)], axis=1), total


def local(mass_bin, mobility_bin, intensity, basis_init, profile_init):
    n_pix = lax.psum(1, "pix")
    n_feat = lax.psum(1, "feat")
    rows = mass_bin.shape[0]
    block = math.gcd(rows, 1024)
    count = rows // block
    spectra = lax.map(
        bin_block,
        (
            mass_bin.reshape(count, block, PEAKS),
            mobility_bin.reshape(count, block, PEAKS),
            intensity.reshape(count, block, PEAKS),
        ),
    )
    spectra = spectra.reshape(rows, MZ * MOB)
    highest = lax.Precision.HIGHEST
    basis, profiles = (basis_init, profile_init)
    for step in range(ITERS):
        partial_h = lax.dot_general(
            basis.astype(jnp.bfloat16),
            spectra,
            (((0,), (0,)), ((), ())),
            preferred_element_type=jnp.float32,
        )
        partial_gram = lax.dot_general(
            basis,
            basis,
            (((0,), (0,)), ((), ())),
            precision=highest,
            preferred_element_type=jnp.float32,
        )
        shared, gram_feat = scatter_once(partial_h, partial_gram, "feat", n_feat)
        both = exchange_sum(jnp.concatenate([shared, gram_feat], axis=1), "pix", n_pix)
        width = shared.shape[1]
        numer_h = both[:, :width]
        gram_w = both[:, width:]
        profiles = (
            profiles
            * numer_h
            / (
                jnp.dot(gram_w, profiles, precision=highest, preferred_element_type=jnp.float32)
                + EPS
            )
        )
        local_gram = lax.dot_general(
            profiles,
            profiles,
            (((1,), (1,)), ((), ())),
            precision=highest,
            preferred_element_type=jnp.float32,
        )
        profiles_all, gram_h = double_gather(profiles.astype(jnp.bfloat16), local_gram, "feat", n_feat)
        numer_w = lax.dot_general(
            spectra,
            profiles_all,
            (((1,), (1,)), ((), ())),
            preferred_element_type=jnp.float32,
        )
        basis = (
            basis
            * numer_w
            / (jnp.dot(basis, gram_h, precision=highest, preferred_element_type=jnp.float32) + EPS)
        )
    return (basis, profiles)


def solution(mesh):
    return jax.shard_map(
        local,
        mesh=mesh,
        in_specs=(
            P(("pix", "feat"), None),
            P(("pix", "feat"), None),
            P(("pix", "feat"), None),
            P(("pix", "feat"), None),
            P(None, "feat"),
        ),
        out_specs=(P(("pix", "feat"), None), P(None, "feat")),
        check_vma=False,
    )
```
